128 devices in a mesh: seq: 32 (over x, y, core), dp: 4 (over z).
Axes of the slice: x: 4, y: 4, z: 4, core: 2. Of those that a mesh axis runs over, the one named last changes fastest.
Arguments:
- inputs: bfloat16 [8, 8192, 1024], P('dp', 'seq'), may hold values from -6 to 6
- lengths: int32 [8, 64], P('dp'), may hold values from 1 to 256, 8192 in all within a row
- norm_gain: float32 [1024], replicated, may hold values from 0.5 to 1.5
- qkv_weight: bfloat16 [1024, 3072], replicated, may hold values from -4 to 4
- out_weight: bfloat16 [1024, 1024], replicated, may hold values from -0.75 to 0.75
- kernel: float32 [31, 1024], replicated, may hold values from -1 to 1
- cotangent: bfloat16 [8, 8192, 1024], P('dp', 'seq'), may hold values from -6 to 6
Outputs:
- output: bfloat16 [8, 8192, 1024], P('dp', 'seq')
- grad_inputs: bfloat16 [8, 8192, 1024], P('dp', 'seq')
- grad_qkv_weight: float32 [1024, 3072], P(('seq', 'dp'))
- grad_out_weight: float32 [1024, 1024], P(('seq', 'dp'))
- grad_kernel: float32 [31, 1024], replicated
- grad_gain: float32 [1024], replicated
The draws below stay inside these ranges and needn't reach their ends.
Inputs may be any that keep to these rules, and one draw needn't show every extreme that they name: `lengths`: each row sums to 8192.
All inputs are finite; a program needn't handle non-finite values.
Results may differ from the reference program's by a relative error of at most 0.017.
Values may be sent and summed in bfloat16 or wider, within the bound.
No kernel may reach another device: no remote copies, remote signals or barrier semaphores. Data moves between devices by JAX's collectives and lax.ppermute only.
A program may use at most 192 MiB of HBM per device.

```python
import math
import jax
import jax.numpy as jnp
import numpy as np
from jax import lax

D = 1024
HEADS = 16
HEAD_DIM = 64
KERNEL = 31
MOST = 256
LENGTH = 8192
BATCH = 8
UTTS = 64


def draw_qkv_weight(key, part):
    first = jax.random.fold_in(key, 0)
    base_rows = jnp.clip(jax.random.normal(first, (D, 3 * D), jnp.float32), -6.0, 6.0) * D ** (-0.5)
    return jnp.clip(base_rows, -4.0, 4.0).astype(jnp.bfloat16)


def level_of(own_key, extent, cuts, low, top_value):
    factor_of = 1.0
    for dim, blocks in cuts:
        heights = jax.random.uniform(jax.random.fold_in(jax.random.fold_in(own_key, 6), dim), (blocks,), jnp.float32, low / len(cuts), top_value / len(cuts))
        factor_of = factor_of * jnp.repeat(jnp.exp(heights), extent[dim] // blocks).reshape((-1,) + (1,) * (len(extent) - 1 - dim))
    return factor_of


def profile(count, total, bound, slope):
    weights = [(1 << 20) // math.isqrt(rank ** slope) + 1 for rank in range(2, count + 1)]
    rest, given = total - bound - (count - 1), [1] * (count - 1)
    while rest > 0:
        free = [i for i in range(count - 1) if given[i] < bound]
        whole, remaining = sum([weights[i] for i in free]), rest
        for i in free:
            extra = min(bound - given[i], max(1, remaining * weights[i] // whole), rest)
            given[i] = given[i] + extra
            rest = rest - extra
    return np.array([bound] + given)


def uneven(rng, number_of, total, bound, slope):
    if number_of == 2:
        one = jax.random.randint(rng, (), max(1, total - bound), min(bound, total - 1) + 1)
        return jnp.stack([one, total - one])
    tallies = jnp.asarray(profile(number_of, total, bound, slope), jnp.int32)
    twos = (number_of - 1) // 2
    donor, sink = tallies[1:1 + 2 * twos:2], tallies[2:2 + 2 * twos:2]
    room = jnp.minimum(donor - 1, bound - sink)
    passed = jax.random.randint(jax.random.fold_in(rng, 1), (twos,), 0, 1 << 20) % (room + 1)
    tallies = tallies.at[1:1 + 2 * twos:2].set(donor - passed).at[2:2 + 2 * twos:2].set(sink + passed)
    return tallies[jax.random.permutation(jax.random.fold_in(rng, 2), number_of)]


def normal_values(stream_key, dims, deviation, most, pieces=(), kind=jnp.bfloat16):
    gain = level_of(stream_key, dims, pieces, -0.22, 0.18) if pieces else 1.0
    result = jax.random.normal(stream_key, dims, jnp.float32) * deviation * gain
    return jnp.minimum(jnp.maximum(result, -most), most).astype(kind)


def setup_inputs(seed: int = 0) -> dict:
    key_list = jax.random.split(jax.random.key(seed), 8)
    return {
        "inputs": normal_values(key_list[0], (BATCH, LENGTH, D), 1.0, 6.0, ((0, 4), (1, 32))),
        "lengths": jax.vmap(lambda own: uneven(own, UTTS, LENGTH, MOST, 2))(jax.random.split(key_list[1], BATCH)).reshape((BATCH, UTTS)).astype(jnp.int32),
        "norm_gain": jnp.clip(1.0 + 0.1 * jax.random.normal(key_list[2], (D,), jnp.float32), 0.5, 1.5),
        "qkv_weight": draw_qkv_weight(jax.random.fold_in(key_list[7], 71), 0),
        "out_weight": normal_values(key_list[4], (D, D), (D // 16) ** -0.5, 0.75),
        "kernel": normal_values(key_list[5], (KERNEL, D), KERNEL ** -0.5, 1.0, (), jnp.float32),
        "cotangent": normal_values(key_list[6], (BATCH, LENGTH, D), 1.0, 6.0, ((0, 4), (1, 32))),
    }


EPSILON = 1e-05
NEGATIVE = -1e+30

def segment_ids(positions, length_row, seq_length):
    ends = jnp.cumsum(length_row).astype(jnp.int32)
    inside = (positions >= 0) & (positions < seq_length)
    counted = lax.optimization_barrier(jnp.sum((ends[None, :] <= positions[:, None]).astype(jnp.int32), axis=1))
    return jnp.where(inside, counted, -1).astype(jnp.int32)

def as_float(value):
    return value.astype(jnp.float32)

def rounded(value):
    return lax.optimization_barrier(value.astype(jnp.bfloat16)).astype(jnp.float32)

def block_probs(queries, key_rows, allowed, score_scale):
    scores = jnp.einsum('hqd,hkd->hqk', as_float(queries), as_float(key_rows)) * score_scale
    scores = jnp.where(allowed[None], scores, NEGATIVE)
    row_max = lax.optimization_barrier(jnp.max(scores, axis=-1, keepdims=True))
    exponent = jnp.where(allowed[None], jnp.exp(scores - row_max), 0.0)
    return exponent / lax.optimization_barrier(jnp.sum(exponent, axis=-1, keepdims=True))

def attention_forward(queries, key_rows, values, segment_all, segment_pad, score_scale):
    block_rows = min(512, LENGTH)
    window = block_rows + 2 * MOST
    pad_keys = jnp.pad(key_rows, ((0, 0), (MOST, MOST), (0, 0)))
    pad_values = jnp.pad(values, ((0, 0), (MOST, MOST), (0, 0)))

    def one_block(step_index):
        offset = step_index * block_rows
        allowed = lax.dynamic_slice_in_dim(segment_all, offset, block_rows, 0)[:, None] == lax.dynamic_slice_in_dim(segment_pad, offset, window, 0)[None, :]
        attn_probs = block_probs(lax.dynamic_slice_in_dim(queries, offset, block_rows, 1), lax.dynamic_slice_in_dim(pad_keys, offset, window, 1), allowed, score_scale)
        value_block = as_float(lax.dynamic_slice_in_dim(pad_values, offset, window, 1))
        return jnp.einsum('hqk,hkd->hqd', rounded(attn_probs), value_block).astype(jnp.bfloat16)
    block_outs = lax.map(one_block, jnp.arange(LENGTH // block_rows, dtype=jnp.int32))
    return block_outs.transpose(1, 0, 2, 3).reshape(HEADS, LENGTH, HEAD_DIM)

def attention_backward(queries, key_rows, values, segment_all, segment_pad, score_scale, output, grad_output):
    block_rows = min(512, LENGTH)
    window = block_rows + 2 * MOST
    pad_keys = jnp.pad(key_rows, ((0, 0), (MOST, MOST), (0, 0)))
    pad_values = jnp.pad(values, ((0, 0), (MOST, MOST), (0, 0)))

    def one_block(carried, step_index):
        key_grads, value_grads = carried
        offset = step_index * block_rows
        allowed = lax.dynamic_slice_in_dim(segment_all, offset, block_rows, 0)[:, None] == lax.dynamic_slice_in_dim(segment_pad, offset, window, 0)[None, :]
        query_block = lax.dynamic_slice_in_dim(queries, offset, block_rows, 1)
        key_block = lax.dynamic_slice_in_dim(pad_keys, offset, window, 1)
        value_block = lax.dynamic_slice_in_dim(pad_values, offset, window, 1)
        out_block = as_float(lax.dynamic_slice_in_dim(output, offset, block_rows, 1))
        grad_block = as_float(lax.dynamic_slice_in_dim(grad_output, offset, block_rows, 1))
        attn_probs = block_probs(query_block, key_block, allowed, score_scale)
        row_delta = lax.optimization_barrier(jnp.sum(grad_block * out_block, axis=-1, keepdims=True))
        value_part = jnp.einsum('hqk,hqd->hkd', rounded(attn_probs), grad_block)
        grad_probs = jnp.einsum('hqd,hkd->hqk', grad_block, as_float(value_block))
        grad_scores = rounded(attn_probs * (grad_probs - row_delta) * score_scale)
        grad_query = jnp.einsum('hqk,hkd->hqd', grad_scores, as_float(key_block)).astype(jnp.bfloat16)
        key_part = jnp.einsum('hqk,hqd->hkd', grad_scores, as_float(query_block))
        key_grads = lax.dynamic_update_slice_in_dim(key_grads, lax.dynamic_slice_in_dim(key_grads, offset, window, 1) + key_part, offset, 1)
        value_grads = lax.dynamic_update_slice_in_dim(value_grads, lax.dynamic_slice_in_dim(value_grads, offset, window, 1) + value_part, offset, 1)
        return ((key_grads, value_grads), grad_query)
    empty_grads = jnp.zeros((HEADS, LENGTH + 2 * MOST, HEAD_DIM), jnp.float32)
    (key_grads, value_grads), query_grads = lax.scan(one_block, (empty_grads, empty_grads), jnp.arange(LENGTH // block_rows, dtype=jnp.int32))
    query_grads = query_grads.transpose(1, 0, 2, 3).reshape(HEADS, LENGTH, HEAD_DIM)
    return (query_grads, key_grads[:, MOST:MOST + LENGTH].astype(jnp.bfloat16), value_grads[:, MOST:MOST + LENGTH].astype(jnp.bfloat16))

def one_batch(batch_args, norm_gain, qkv_weight, out_weight, kernel):
    inputs, length_row, cotangent = batch_args
    conv_reach = KERNEL // 2
    score_scale = HEAD_DIM ** (-0.5)
    widened = as_float(inputs)
    average = lax.optimization_barrier(jnp.mean(widened, axis=-1, keepdims=True))
    centred = widened - average
    inverse = lax.rsqrt(lax.optimization_barrier(jnp.mean(centred * centred, axis=-1, keepdims=True)) + EPSILON)
    unit_rows = centred * inverse
    normed = (unit_rows * norm_gain).astype(jnp.bfloat16)
    projected = jnp.dot(normed, qkv_weight, preferred_element_type=jnp.float32).astype(jnp.bfloat16)
    head_split = projected.reshape(LENGTH, 3, HEADS, HEAD_DIM).transpose(1, 2, 0, 3)
    segment_all = segment_ids(jnp.arange(LENGTH, dtype=jnp.int32), length_row, LENGTH)
    segment_pad = segment_ids(jnp.arange(-MOST, LENGTH + MOST, dtype=jnp.int32), length_row, LENGTH)
    head_out = attention_forward(head_split[0], head_split[1], head_split[2], segment_all, segment_pad, score_scale)
    attended = head_out.transpose(1, 0, 2).reshape(LENGTH, D)
    hidden = (widened + jnp.dot(attended, out_weight, preferred_element_type=jnp.float32)).astype(jnp.bfloat16)
    padded = as_float(jnp.pad(hidden, ((conv_reach, conv_reach), (0, 0))))
    segment_rim = segment_ids(jnp.arange(-conv_reach, LENGTH + conv_reach, dtype=jnp.int32), length_row, LENGTH)
    conv_sum = jnp.zeros((LENGTH, D), jnp.float32)
    for tap_index in range(KERNEL):
        same_seg = (segment_rim[tap_index:tap_index + LENGTH] == segment_all)[:, None]
        conv_sum = conv_sum + jnp.where(same_seg, kernel[tap_index] * padded[tap_index:tap_index + LENGTH], 0.0)
    gated = jax.nn.sigmoid(conv_sum)
    output = (as_float(hidden) + conv_sum * gated).astype(jnp.bfloat16)
    incoming = as_float(cotangent)
    grad_conv = incoming * gated * (1.0 + conv_sum * (1.0 - gated))
    grad_pad = jnp.pad(grad_conv, ((conv_reach, conv_reach), (0, 0)))
    grad_hidden = incoming
    kernel_rows = []
    for tap_index in range(KERNEL):
        back_index = 2 * conv_reach - tap_index
        same_back = (segment_rim[back_index:back_index + LENGTH] == segment_all)[:, None]
        grad_hidden = grad_hidden + jnp.where(same_back, kernel[tap_index] * grad_pad[back_index:back_index + LENGTH], 0.0)
        same_seg = (segment_rim[tap_index:tap_index + LENGTH] == segment_all)[:, None]
        kernel_rows.append(lax.optimization_barrier(jnp.sum(jnp.where(same_seg, grad_conv * padded[tap_index:tap_index + LENGTH], 0.0), axis=0)))
    grad_hidden_b = grad_hidden.astype(jnp.bfloat16)
    grad_attended = jnp.dot(grad_hidden_b, out_weight.T, preferred_element_type=jnp.float32).astype(jnp.bfloat16)
    grad_heads = grad_attended.reshape(LENGTH, HEADS, HEAD_DIM).transpose(1, 0, 2)
    query_grads, key_grads, value_grads = attention_backward(head_split[0], head_split[1], head_split[2], segment_all, segment_pad, score_scale, head_out, grad_heads)
    grad_qkv = jnp.stack([query_grads, key_grads, value_grads]).transpose(2, 0, 1, 3).reshape(LENGTH, 3 * D)
    grad_normed = jnp.dot(grad_qkv, qkv_weight.T, preferred_element_type=jnp.float32)
    scaled = grad_normed * norm_gain
    grad_inputs = grad_hidden + inverse * (scaled - lax.optimization_barrier(jnp.mean(scaled, axis=-1, keepdims=True)) - unit_rows * lax.optimization_barrier(jnp.mean(scaled * unit_rows, axis=-1, keepdims=True)))
    gain_sum = lax.optimization_barrier(jnp.sum(grad_normed * unit_rows, axis=0))
    qkv_sum = jnp.dot(normed.T, grad_qkv, preferred_element_type=jnp.float32)
    out_sum = jnp.dot(attended.T, grad_hidden_b, preferred_element_type=jnp.float32)
    return (output, grad_inputs.astype(jnp.bfloat16), qkv_sum, out_sum, jnp.stack(kernel_rows), gain_sum)

def reference(inputs, lengths, norm_gain, qkv_weight, out_weight, kernel, cotangent):

    def per_batch(batch_args):
        return one_batch(batch_args, norm_gain, qkv_weight, out_weight, kernel)
    results = lax.map(per_batch, (inputs, lengths, cotangent))
    factor = (BATCH * LENGTH) ** (-0.5)
    return (results[0], results[1], lax.optimization_barrier(jnp.sum(results[2], axis=0)) * factor, lax.optimization_barrier(jnp.sum(results[3], axis=0)) * factor, lax.optimization_barrier(jnp.sum(results[4], axis=0)) * factor, lax.optimization_barrier(jnp.sum(results[5], axis=0)) * factor)
```

```python
import jax
import jax.numpy as jnp
from jax import lax
from jax.sharding import PartitionSpec as P

HEADS = 16
MOST = 256


EPSILON = 1e-05
NEGATIVE = -1e30


def with_halo(shard, sides, width):
    for axis, dim in sides:
        size, length = (lax.axis_size(axis), shard.shape[dim])
        up = [(i, (i + 1) % size) for i in range(size - 1)]
        down = [(j, i) for i, j in up]
        last = lax.slice_in_dim(shard, length - width, length, axis=dim)
        initial = lax.slice_in_dim(shard, 0, width, axis=dim)
        before = lax.ppermute(last, axis, up)
        after = lax.ppermute(initial, axis, down)
        shard = jnp.concatenate([before, shard, after], axis=dim)
    return shard


def staged_scatter(partial):
    partial = lax.psum_scatter(partial, "seq", scatter_dimension=0, tiled=True)
    return lax.psum_scatter(partial, "dp", scatter_dimension=0, tiled=True)


def segment_ids(positions, length_row, seq_length):
    ends = jnp.cumsum(length_row)
    inside = (positions >= 0) & (positions < seq_length)
    counted = jnp.sum((ends[None, :] <= positions[:, None]).astype(jnp.int32), axis=1)
    return jnp.where(inside, counted, -1)


def block_probs(queries, key_rows, allowed, score_scale):
    scores = (
        jnp.einsum("hqd,hkd->hqk", queries, key_rows, preferred_element_type=jnp.float32)
        * score_scale
    )
    scores = jnp.where(allowed[None], scores, NEGATIVE)
    row_max = jnp.max(scores, axis=-1, keepdims=True)
    exponent = jnp.where(allowed[None], jnp.exp(scores - row_max), 0.0)
    return exponent / jnp.sum(exponent, axis=-1, keepdims=True)


def block_forward(queries, key_rows, values, allowed, score_scale):
    attn_probs = block_probs(queries, key_rows, allowed, score_scale)
    return jnp.einsum(
        "hqk,hkd->hqd", attn_probs.astype(jnp.bfloat16), values, preferred_element_type=jnp.float32
    ).astype(jnp.bfloat16)


def block_backward(queries, key_rows, values, allowed, score_scale, output, grad_output):
    attn_probs = block_probs(queries, key_rows, allowed, score_scale)
    row_delta = jnp.sum(
        grad_output.astype(jnp.float32) * output.astype(jnp.float32), axis=-1, keepdims=True
    )
    value_part = jnp.einsum(
        "hqk,hqd->hkd",
        attn_probs.astype(jnp.bfloat16),
        grad_output,
        preferred_element_type=jnp.float32,
    )
    grad_probs = jnp.einsum("hqd,hkd->hqk", grad_output, values, preferred_element_type=jnp.float32)
    grad_scores = (attn_probs * (grad_probs - row_delta) * score_scale).astype(jnp.bfloat16)
    grad_query = jnp.einsum(
        "hqk,hkd->hqd", grad_scores, key_rows, preferred_element_type=jnp.float32
    ).astype(jnp.bfloat16)
    key_part = jnp.einsum("hqk,hqd->hkd", grad_scores, queries, preferred_element_type=jnp.float32)
    return (grad_query, key_part, value_part)


def windowed_forward(queries, key_rows, values, segment_all, segment_pad, score_scale):
    pair_count, seq_length, head_dim = queries.shape
    block_rows = min(512, seq_length)
    window = block_rows + 2 * MOST
    pad_keys = jnp.pad(key_rows, ((0, 0), (MOST, MOST), (0, 0)))
    pad_values = jnp.pad(values, ((0, 0), (MOST, MOST), (0, 0)))

    def one_block(step_index):
        offset = step_index * block_rows
        allowed = (
            lax.dynamic_slice_in_dim(segment_all, offset, block_rows, 0)[:, None]
            == lax.dynamic_slice_in_dim(segment_pad, offset, window, 0)[None, :]
        )
        return block_forward(
            lax.dynamic_slice_in_dim(queries, offset, block_rows, 1),
            lax.dynamic_slice_in_dim(pad_keys, offset, window, 1),
            lax.dynamic_slice_in_dim(pad_values, offset, window, 1),
            allowed,
            score_scale,
        )

    block_outs = lax.map(one_block, jnp.arange(seq_length // block_rows, dtype=jnp.int32))
    return block_outs.transpose(1, 0, 2, 3).reshape(pair_count, seq_length, head_dim)


def windowed_backward(
    queries, key_rows, values, segment_all, segment_pad, score_scale, output, grad_output
):
    pair_count, seq_length, head_dim = queries.shape
    block_rows = min(512, seq_length)
    window = block_rows + 2 * MOST
    pad_keys = jnp.pad(key_rows, ((0, 0), (MOST, MOST), (0, 0)))
    pad_values = jnp.pad(values, ((0, 0), (MOST, MOST), (0, 0)))

    def one_block(carried, step_index):
        key_grads, value_grads = carried
        offset = step_index * block_rows
        allowed = (
            lax.dynamic_slice_in_dim(segment_all, offset, block_rows, 0)[:, None]
            == lax.dynamic_slice_in_dim(segment_pad, offset, window, 0)[None, :]
        )
        grad_query, key_part, value_part = block_backward(
            lax.dynamic_slice_in_dim(queries, offset, block_rows, 1),
            lax.dynamic_slice_in_dim(pad_keys, offset, window, 1),
            lax.dynamic_slice_in_dim(pad_values, offset, window, 1),
            allowed,
            score_scale,
            lax.dynamic_slice_in_dim(output, offset, block_rows, 1),
            lax.dynamic_slice_in_dim(grad_output, offset, block_rows, 1),
        )
        key_grads = lax.dynamic_update_slice_in_dim(
            key_grads, lax.dynamic_slice_in_dim(key_grads, offset, window, 1) + key_part, offset, 1
        )
        value_grads = lax.dynamic_update_slice_in_dim(
            value_grads,
            lax.dynamic_slice_in_dim(value_grads, offset, window, 1) + value_part,
            offset,
            1,
        )
        return ((key_grads, value_grads), grad_query)

    empty_grads = jnp.zeros((pair_count, seq_length + 2 * MOST, head_dim), jnp.float32)
    (key_grads, value_grads), query_grads = lax.scan(
        one_block, (empty_grads, empty_grads), jnp.arange(seq_length // block_rows, dtype=jnp.int32)
    )
    query_grads = query_grads.transpose(1, 0, 2, 3).reshape(pair_count, seq_length, head_dim)
    return (
        query_grads,
        key_grads[:, MOST : MOST + seq_length].astype(jnp.bfloat16),
        value_grads[:, MOST : MOST + seq_length].astype(jnp.bfloat16),
    )


def local(inputs, lengths, norm_gain, qkv_weight, out_weight, kernel, cotangent):
    batches, frames, model_width = inputs.shape
    shards = lax.axis_size("seq")
    position = lax.axis_index("seq")
    seq_length = frames * shards
    head_dim = model_width // HEADS
    score_scale = head_dim ** (-0.5)
    conv_reach = kernel.shape[0] // 2
    factor = (batches * seq_length * lax.axis_size("dp")) ** (-0.5)
    first_frame = position * frames
    local_pos = first_frame + jnp.arange(frames, dtype=jnp.int32)
    segment_local = jnp.stack(
        [segment_ids(local_pos, lengths[batch_index], seq_length) for batch_index in range(batches)]
    )
    widened = inputs.astype(jnp.float32)
    average = jnp.mean(widened, axis=-1, keepdims=True)
    centred = widened - average
    inverse = lax.rsqrt(jnp.mean(centred * centred, axis=-1, keepdims=True) + EPSILON)
    unit_rows = centred * inverse
    normed = (unit_rows * norm_gain).astype(jnp.bfloat16)
    flat_normed = normed.reshape(-1, model_width)
    projected = jnp.dot(flat_normed, qkv_weight, preferred_element_type=jnp.float32).astype(
        jnp.bfloat16
    )
    projected = projected.reshape(batches, frames, 3 * model_width)
    pair_count = batches * HEADS // shards
    packed = projected.reshape(batches, frames, 3, HEADS, head_dim).transpose(0, 3, 1, 2, 4)
    packed = packed.reshape(batches * HEADS, frames // 2, 6 * head_dim)
    gathered = lax.all_to_all(packed, "seq", split_axis=0, concat_axis=1, tiled=True).reshape(
        pair_count, seq_length, 3, head_dim
    )
    head_queries = gathered[:, :, 0]
    head_keys = gathered[:, :, 1]
    head_values = gathered[:, :, 2]
    local_batch = position * pair_count // HEADS
    length_row = lax.dynamic_index_in_dim(lengths, local_batch, 0, keepdims=False)
    segment_all = segment_ids(jnp.arange(seq_length, dtype=jnp.int32), length_row, seq_length)
    segment_pad = segment_ids(
        jnp.arange(-MOST, seq_length + MOST, dtype=jnp.int32), length_row, seq_length
    )
    head_out = windowed_forward(
        head_queries, head_keys, head_values, segment_all, segment_pad, score_scale
    )
    returned = lax.all_to_all(
        head_out.reshape(pair_count, seq_length // 2, 2 * head_dim),
        "seq",
        split_axis=1,
        concat_axis=0,
        tiled=True,
    )
    attended = returned.reshape(batches, HEADS, frames, head_dim).transpose(0, 2, 1, 3)
    attended = attended.reshape(batches, frames, model_width)
    flat_attended = attended.reshape(-1, model_width)
    attn_rows = jnp.dot(flat_attended, out_weight, preferred_element_type=jnp.float32)
    hidden = (widened + attn_rows.reshape(batches, frames, model_width)).astype(jnp.bfloat16)
    padded = with_halo(hidden, (("seq", 1),), conv_reach).astype(jnp.float32)
    ext_pos = first_frame - conv_reach + jnp.arange(frames + 2 * conv_reach, dtype=jnp.int32)
    segment_ext = jnp.stack(
        [segment_ids(ext_pos, lengths[batch_index], seq_length) for batch_index in range(batches)]
    )
    conv_sum = jnp.zeros((batches, frames, model_width), jnp.float32)
    for tap_index in range(kernel.shape[0]):
        same_seg = (segment_ext[:, tap_index : tap_index + frames] == segment_local)[..., None]
        conv_sum = conv_sum + jnp.where(
            same_seg, kernel[tap_index] * padded[:, tap_index : tap_index + frames], 0.0
        )
    gated = jax.nn.sigmoid(conv_sum)
    output = (hidden.astype(jnp.float32) + conv_sum * gated).astype(jnp.bfloat16)
    incoming = cotangent.astype(jnp.float32)
    grad_conv = incoming * gated * (1.0 + conv_sum * (1.0 - gated))
    grad_pad = with_halo(grad_conv.astype(jnp.bfloat16), (("seq", 1),), conv_reach).astype(
        grad_conv.dtype
    )
    grad_hidden = incoming
    kernel_rows = []
    for tap_index in range(kernel.shape[0]):
        back_index = 2 * conv_reach - tap_index
        same_back = (segment_ext[:, back_index : back_index + frames] == segment_local)[..., None]
        grad_hidden = grad_hidden + jnp.where(
            same_back, kernel[tap_index] * grad_pad[:, back_index : back_index + frames], 0.0
        )
        same_seg = (segment_ext[:, tap_index : tap_index + frames] == segment_local)[..., None]
        kernel_rows.append(
            jnp.sum(
                jnp.where(same_seg, grad_conv * padded[:, tap_index : tap_index + frames], 0.0),
                axis=(0, 1),
            )
        )
    grad_hidden_b = grad_hidden.astype(jnp.bfloat16)
    flat_grad_hidden = grad_hidden_b.reshape(-1, model_width)
    grad_attended = jnp.dot(
        flat_grad_hidden, out_weight.T, preferred_element_type=jnp.float32
    ).astype(jnp.bfloat16)
    grad_packed = grad_attended.reshape(batches, frames, HEADS, head_dim).transpose(0, 2, 1, 3)
    grad_packed = grad_packed.reshape(batches * HEADS, frames // 2, 2 * head_dim)
    grad_heads = lax.all_to_all(
        grad_packed, "seq", split_axis=0, concat_axis=1, tiled=True
    ).reshape(pair_count, seq_length, head_dim)
    query_grads, key_grads, value_grads = windowed_backward(
        head_queries,
        head_keys,
        head_values,
        segment_all,
        segment_pad,
        score_scale,
        head_out,
        grad_heads,
    )
    stacked = jnp.stack([query_grads, key_grads, value_grads], axis=2).reshape(
        pair_count, seq_length // 2, 6 * head_dim
    )
    sent_back = lax.all_to_all(stacked, "seq", split_axis=1, concat_axis=0, tiled=True)
    grad_qkv = sent_back.reshape(batches, HEADS, frames, 3, head_dim).transpose(0, 2, 3, 1, 4)
    grad_qkv = grad_qkv.reshape(batches, frames, 3 * model_width)
    flat_grad_qkv = grad_qkv.reshape(-1, 3 * model_width)
    grad_normed = jnp.dot(flat_grad_qkv, qkv_weight.T, preferred_element_type=jnp.float32)
    grad_normed = grad_normed.reshape(batches, frames, model_width)
    scaled = grad_normed * norm_gain
    grad_inputs = grad_hidden + inverse * (
        scaled
        - jnp.mean(scaled, axis=-1, keepdims=True)
        - unit_rows * jnp.mean(scaled * unit_rows, axis=-1, keepdims=True)
    )
    gain_sum = jnp.sum(grad_normed * unit_rows, axis=(0, 1))
    contract_rows = (((0,), (0,)), ((), ()))
    out_sum = staged_scatter(
        lax.dot_general(
            flat_attended, flat_grad_hidden, contract_rows, preferred_element_type=jnp.float32
        )
    )
    qkv_sum = staged_scatter(
        lax.dot_general(flat_normed, flat_grad_qkv, contract_rows, preferred_element_type=jnp.float32)
    )
    small_sums = lax.psum((jnp.stack(kernel_rows), gain_sum), ("seq", "dp"))
    return (
        output,
        grad_inputs.astype(jnp.bfloat16),
        qkv_sum * factor,
        out_sum * factor,
        small_sums[0] * factor,
        small_sums[1] * factor,
    )


def solution(mesh):
    in_specs = (P("dp", "seq", None), P("dp", None), P(), P(), P(), P(), P("dp", "seq", None))
    out_specs = (
        P("dp", "seq", None),
        P("dp", "seq", None),
        P(("seq", "dp"), None),
        P(("seq", "dp"), None),
        P(),
        P(),
    )
    return jax.shard_map(local, mesh=mesh, in_specs=in_specs, out_specs=out_specs, check_vma=False)
```

```python
import jax
import jax.numpy as jnp
from jax import lax
from jax.sharding import PartitionSpec as P

HEADS = 16
MOST = 256


EPSILON = 1e-05
NEGATIVE = -1e30


def with_halo(shard, sides, width):
    for axis, dim in sides:
        size, length = (lax.axis_size(axis), shard.shape[dim])
        up = [(i, (i + 1) % size) for i in range(size - 1)]
        down = [(j, i) for i, j in up]
        last = lax.slice_in_dim(shard, length - width, length, axis=dim)
        initial = lax.slice_in_dim(shard, 0, width, axis=dim)
        before = lax.ppermute(last, axis, up)
        after = lax.ppermute(initial, axis, down)
        shard = jnp.concatenate([before, shard, after], axis=dim)
    return shard


def staged_scatter(partial):
    partial = lax.psum_scatter(partial, "seq", scatter_dimension=0, tiled=True)
    return lax.psum_scatter(partial, "dp", scatter_dimension=0, tiled=True)


def segment_ids(positions, length_row, seq_length):
    ends = jnp.cumsum(length_row)
    inside = (positions >= 0) & (positions < seq_length)
    counted = jnp.sum((ends[None, :] <= positions[:, None]).astype(jnp.int32), axis=1)
    return jnp.where(inside, counted, -1)


def from_neighbour(shard, axis, step):
    size = lax.axis_size(axis)
    if step > 0:
        pairs = [(i, i + step) for i in range(size - step)]
    else:
        pairs = [(i - step, i) for i in range(size + step)]
    return lax.ppermute(shard, axis, pairs)


def local(inputs, lengths, norm_gain, qkv_weight, out_weight, kernel, cotangent):
    batches, frames, model_width = inputs.shape
    shards = lax.axis_size("seq")
    position = lax.axis_index("seq")
    seq_length = frames * shards
    head_dim = model_width // HEADS
    score_scale = head_dim ** (-0.5)
    conv_reach = kernel.shape[0] // 2
    factor = (batches * seq_length * lax.axis_size("dp")) ** (-0.5)
    first_frame = position * frames
    local_pos = first_frame + jnp.arange(frames, dtype=jnp.int32)
    segment_local = jnp.stack(
        [segment_ids(local_pos, lengths[batch_index], seq_length) for batch_index in range(batches)]
    )
    widened = inputs.astype(jnp.float32)
    average = jnp.mean(widened, axis=-1, keepdims=True)
    centred = widened - average
    inverse = lax.rsqrt(jnp.mean(centred * centred, axis=-1, keepdims=True) + EPSILON)
    unit_rows = centred * inverse
    normed = (unit_rows * norm_gain).astype(jnp.bfloat16)
    flat_normed = normed.reshape(-1, model_width)
    projected = jnp.dot(flat_normed, qkv_weight, preferred_element_type=jnp.float32).astype(
        jnp.bfloat16
    )
    projected = projected.reshape(batches, frames, 3 * model_width)
    proj5 = projected.reshape(batches, frames, 3, HEADS, head_dim)
    head_queries = proj5[:, :, 0]
    own_kv = proj5[:, :, 1:]
    kv_window = jnp.concatenate(
        [from_neighbour(own_kv, "seq", 1), own_kv, from_neighbour(own_kv, "seq", -1)], axis=1
    )
    head_keys = kv_window[:, :, 0]
    head_values = kv_window[:, :, 1]
    window_pos = first_frame - frames + jnp.arange(3 * frames, dtype=jnp.int32)
    segment_window = jnp.stack(
        [segment_ids(window_pos, lengths[batch_index], seq_length) for batch_index in range(batches)]
    )
    allowed = (segment_local[:, :, None] == segment_window[:, None, :])[:, None]
    scores = (
        jnp.einsum("bqhd,bkhd->bhqk", head_queries, head_keys, preferred_element_type=jnp.float32)
        * score_scale
    )
    scores = jnp.where(allowed, scores, NEGATIVE)
    row_max = jnp.max(scores, axis=-1, keepdims=True)
    exponent = jnp.where(allowed, jnp.exp(scores - row_max), 0.0)
    attn_probs = exponent / jnp.sum(exponent, axis=-1, keepdims=True)
    weights = attn_probs.astype(jnp.bfloat16)
    head_out = jnp.einsum(
        "bhqk,bkhd->bqhd", weights, head_values, preferred_element_type=jnp.float32
    ).astype(jnp.bfloat16)
    attended = head_out.reshape(batches, frames, model_width)
    flat_attended = attended.reshape(-1, model_width)
    attn_rows = jnp.dot(flat_attended, out_weight, preferred_element_type=jnp.float32)
    hidden = (widened + attn_rows.reshape(batches, frames, model_width)).astype(jnp.bfloat16)
    padded = with_halo(hidden, (("seq", 1),), conv_reach).astype(jnp.float32)
    ext_pos = first_frame - conv_reach + jnp.arange(frames + 2 * conv_reach, dtype=jnp.int32)
    segment_ext = jnp.stack(
        [segment_ids(ext_pos, lengths[batch_index], seq_length) for batch_index in range(batches)]
    )
    conv_sum = jnp.zeros((batches, frames, model_width), jnp.float32)
    for tap_index in range(kernel.shape[0]):
        same_seg = (segment_ext[:, tap_index : tap_index + frames] == segment_local)[..., None]
        conv_sum = conv_sum + jnp.where(
            same_seg, kernel[tap_index] * padded[:, tap_index : tap_index + frames], 0.0
        )
    gated = jax.nn.sigmoid(conv_sum)
    output = (hidden.astype(jnp.float32) + conv_sum * gated).astype(jnp.bfloat16)
    incoming = cotangent.astype(jnp.float32)
    grad_conv = incoming * gated * (1.0 + conv_sum * (1.0 - gated))
    grad_pad = with_halo(grad_conv.astype(jnp.bfloat16), (("seq", 1),), conv_reach).astype(
        grad_conv.dtype
    )
    grad_hidden = incoming
    kernel_rows = []
    for tap_index in range(kernel.shape[0]):
        back_index = 2 * conv_reach - tap_index
        same_back = (segment_ext[:, back_index : back_index + frames] == segment_local)[..., None]
        grad_hidden = grad_hidden + jnp.where(
            same_back, kernel[tap_index] * grad_pad[:, back_index : back_index + frames], 0.0
        )
        same_seg = (segment_ext[:, tap_index : tap_index + frames] == segment_local)[..., None]
        kernel_rows.append(
            jnp.sum(
                jnp.where(same_seg, grad_conv * padded[:, tap_index : tap_index + frames], 0.0),
                axis=(0, 1),
            )
        )
    grad_hidden_b = grad_hidden.astype(jnp.bfloat16)
    flat_grad_hidden = grad_hidden_b.reshape(-1, model_width)
    grad_attended = jnp.dot(
        flat_grad_hidden, out_weight.T, preferred_element_type=jnp.float32
    ).astype(jnp.bfloat16)
    grad_heads = grad_attended.reshape(batches, frames, HEADS, head_dim)
    row_delta = jnp.sum(
        grad_heads.astype(jnp.float32) * head_out.astype(jnp.float32), axis=-1
    ).transpose(0, 2, 1)[..., None]
    value_window = jnp.einsum(
        "bhqk,bqhd->bkhd", weights, grad_heads, preferred_element_type=jnp.float32
    )
    grad_probs = jnp.einsum(
        "bqhd,bkhd->bhqk", grad_heads, head_values, preferred_element_type=jnp.float32
    )
    grad_scores = (attn_probs * (grad_probs - row_delta) * score_scale).astype(jnp.bfloat16)
    query_grads = jnp.einsum(
        "bhqk,bkhd->bqhd", grad_scores, head_keys, preferred_element_type=jnp.float32
    ).astype(jnp.bfloat16)
    key_window = jnp.einsum(
        "bhqk,bqhd->bkhd", grad_scores, head_queries, preferred_element_type=jnp.float32
    )
    kv_grad_window = jnp.stack([key_window, value_window], axis=2)
    kv_grads = (
        kv_grad_window[:, frames : 2 * frames]
        + from_neighbour(kv_grad_window[:, :frames].astype(jnp.bfloat16), "seq", -1).astype(
            jnp.float32
        )
        + from_neighbour(kv_grad_window[:, 2 * frames :].astype(jnp.bfloat16), "seq", 1).astype(
            jnp.float32
        )
    ).astype(jnp.bfloat16)
    grad_qkv = jnp.concatenate([query_grads[:, :, None], kv_grads], axis=2)
    grad_qkv = grad_qkv.reshape(batches, frames, 3 * model_width)
    flat_grad_qkv = grad_qkv.reshape(-1, 3 * model_width)
    grad_normed = jnp.dot(flat_grad_qkv, qkv_weight.T, preferred_element_type=jnp.float32)
    grad_normed = grad_normed.reshape(batches, frames, model_width)
    scaled = grad_normed * norm_gain
    grad_inputs = grad_hidden + inverse * (
        scaled
        - jnp.mean(scaled, axis=-1, keepdims=True)
        - unit_rows * jnp.mean(scaled * unit_rows, axis=-1, keepdims=True)
    )
    gain_sum = jnp.sum(grad_normed * unit_rows, axis=(0, 1))
    contract_rows = (((0,), (0,)), ((), ()))
    out_sum = staged_scatter(
        lax.dot_general(
            flat_attended, flat_grad_hidden, contract_rows, preferred_element_type=jnp.float32
        )
    )
    qkv_sum = staged_scatter(
        lax.dot_general(flat_normed, flat_grad_qkv, contract_rows, preferred_element_type=jnp.float32)
    )
    small_sums = lax.psum((jnp.stack(kernel_rows), gain_sum), ("seq", "dp"))
    return (
        output,
        grad_inputs.astype(jnp.bfloat16),
        qkv_sum * factor,
        out_sum * factor,
        small_sums[0] * factor,
        small_sums[1] * factor,
    )


def solution(mesh):
    in_specs = (P("dp", "seq", None), P("dp", None), P(), P(), P(), P(), P("dp", "seq", None))
    out_specs = (
        P("dp", "seq", None),
        P("dp", "seq", None),
        P(("seq", "dp"), None),
        P(("seq", "dp"), None),
        P(),
        P(),
    )
    return jax.shard_map(local, mesh=mesh, in_specs=in_specs, out_specs=out_specs, check_vma=False)
```

```python
import jax
import jax.numpy as jnp
from jax import lax
from jax.sharding import PartitionSpec as P

HEADS = 16
MOST = 256


EPSILON = 1e-05
NEGATIVE = -1e30


def with_halo(shard, sides, width):
    for axis, dim in sides:
        size, length = (lax.axis_size(axis), shard.shape[dim])
        up = [(i, (i + 1) % size) for i in range(size - 1)]
        down = [(j, i) for i, j in up]
        last = lax.slice_in_dim(shard, length - width, length, axis=dim)
        initial = lax.slice_in_dim(shard, 0, width, axis=dim)
        before = lax.ppermute(last, axis, up)
        after = lax.ppermute(initial, axis, down)
        shard = jnp.concatenate([before, shard, after], axis=dim)
    return shard


def staged_scatter(partial):
    partial = lax.psum_scatter(partial, "seq", scatter_dimension=0, tiled=True)
    return lax.psum_scatter(partial, "dp", scatter_dimension=0, tiled=True)


def segment_ids(positions, length_row, seq_length):
    ends = jnp.cumsum(length_row)
    inside = (positions >= 0) & (positions < seq_length)
    counted = jnp.sum((ends[None, :] <= positions[:, None]).astype(jnp.int32), axis=1)
    return jnp.where(inside, counted, -1)


def from_neighbour(shard, axis, step):
    size = lax.axis_size(axis)
    if step > 0:
        pairs = [(i, i + step) for i in range(size - step)]
    else:
        pairs = [(i - step, i) for i in range(size + step)]
    return lax.ppermute(shard, axis, pairs)


def local(inputs, lengths, norm_gain, qkv_weight, out_weight, kernel, cotangent):
    batches, frames, model_width = inputs.shape
    shards = lax.axis_size("seq")
    position = lax.axis_index("seq")
    seq_length = frames * shards
    head_dim = model_width // HEADS
    score_scale = head_dim ** (-0.5)
    conv_reach = kernel.shape[0] // 2
    factor = (batches * seq_length * lax.axis_size("dp")) ** (-0.5)
    first_frame = position * frames
    local_pos = first_frame + jnp.arange(frames, dtype=jnp.int32)
    segment_local = jnp.stack(
        [segment_ids(local_pos, lengths[batch_index], seq_length) for batch_index in range(batches)]
    )
    widened = inputs.astype(jnp.float32)
    average = jnp.mean(widened, axis=-1, keepdims=True)
    centred = widened - average
    inverse = lax.rsqrt(jnp.mean(centred * centred, axis=-1, keepdims=True) + EPSILON)
    unit_rows = centred * inverse
    normed = (unit_rows * norm_gain).astype(jnp.bfloat16)
    flat_normed = normed.reshape(-1, model_width)
    projected = jnp.dot(flat_normed, qkv_weight, preferred_element_type=jnp.float32).astype(
        jnp.bfloat16
    )
    projected = projected.reshape(batches, frames, 3 * model_width)
    proj5 = projected.reshape(batches, frames, 3, HEADS, head_dim)
    head_queries = proj5[:, :, 0]
    own_kv = proj5[:, :, 1:]
    kv_window = jnp.concatenate(
        [from_neighbour(own_kv, "seq", 1), own_kv, from_neighbour(own_kv, "seq", -1)], axis=1
    )
    head_keys = kv_window[:, :, 0]
    head_values = kv_window[:, :, 1]
    window_pos = first_frame - frames + jnp.arange(3 * frames, dtype=jnp.int32)
    segment_window = jnp.stack(
        [segment_ids(window_pos, lengths[batch_index], seq_length) for batch_index in range(batches)]
    )
    allowed = (segment_local[:, :, None] == segment_window[:, None, :])[:, None]
    scores = (
        jnp.einsum("bqhd,bkhd->bhqk", head_queries, head_keys, preferred_element_type=jnp.float32)
        * score_scale
    )
    scores = jnp.where(allowed, scores, NEGATIVE)
    row_max = jnp.max(scores, axis=-1, keepdims=True)
    exponent = jnp.where(allowed, jnp.exp(scores - row_max), 0.0)
    attn_probs = exponent / jnp.sum(exponent, axis=-1, keepdims=True)
    weights = attn_probs.astype(jnp.bfloat16)
    head_out = jnp.einsum(
        "bhqk,bkhd->bqhd", weights, head_values, preferred_element_type=jnp.float32
    ).astype(jnp.bfloat16)
    attended = head_out.reshape(batches, frames, model_width)
    flat_attended = attended.reshape(-1, model_width)
    attn_rows = jnp.dot(flat_attended, out_weight, preferred_element_type=jnp.float32)
    hidden = (widened + attn_rows.reshape(batches, frames, model_width)).astype(jnp.bfloat16)
    padded = with_halo(hidden, (("seq", 1),), conv_reach).astype(jnp.float32)
    ext_pos = first_frame - conv_reach + jnp.arange(frames + 2 * conv_reach, dtype=jnp.int32)
    segment_ext = jnp.stack(
        [segment_ids(ext_pos, lengths[batch_index], seq_length) for batch_index in range(batches)]
    )
    conv_sum = jnp.zeros((batches, frames, model_width), jnp.float32)
    for tap_index in range(kernel.shape[0]):
        same_seg = (segment_ext[:, tap_index : tap_index + frames] == segment_local)[..., None]
        conv_sum = conv_sum + jnp.where(
            same_seg, kernel[tap_index] * padded[:, tap_index : tap_index + frames], 0.0
        )
    gated = jax.nn.sigmoid(conv_sum)
    output = (hidden.astype(jnp.float32) + conv_sum * gated).astype(jnp.bfloat16)
    incoming = cotangent.astype(jnp.float32)
    grad_conv = incoming * gated * (1.0 + conv_sum * (1.0 - gated))
    grad_pad = with_halo(grad_conv.astype(jnp.bfloat16), (("seq", 1),), conv_reach).astype(
        grad_conv.dtype
    )
    grad_hidden = incoming
    kernel_rows = []
    for tap_index in range(kernel.shape[0]):
        back_index = 2 * conv_reach - tap_index
        same_back = (segment_ext[:, back_index : back_index + frames] == segment_local)[..., None]
        grad_hidden = grad_hidden + jnp.where(
            same_back, kernel[tap_index] * grad_pad[:, back_index : back_index + frames], 0.0
        )
        same_seg = (segment_ext[:, tap_index : tap_index + frames] == segment_local)[..., None]
        kernel_rows.append(
            jnp.sum(
                jnp.where(same_seg, grad_conv * padded[:, tap_index : tap_index + frames], 0.0),
                axis=(0, 1),
            )
        )
    grad_hidden_b = grad_hidden.astype(jnp.bfloat16)
    flat_grad_hidden = grad_hidden_b.reshape(-1, model_width)
    grad_attended = jnp.dot(
        flat_grad_hidden, out_weight.T, preferred_element_type=jnp.float32
    ).astype(jnp.bfloat16)
    grad_heads = grad_attended.reshape(batches, frames, HEADS, head_dim)
    row_delta = jnp.sum(
        grad_heads.astype(jnp.float32) * head_out.astype(jnp.float32), axis=-1
    ).transpose(0, 2, 1)[..., None]
    value_window = jnp.einsum(
        "bhqk,bqhd->bkhd", weights, grad_heads, preferred_element_type=jnp.float32
    )
    grad_probs = jnp.einsum(
        "bqhd,bkhd->bhqk", grad_heads, head_values, preferred_element_type=jnp.float32
    )
    grad_scores = (attn_probs * (grad_probs - row_delta) * score_scale).astype(jnp.bfloat16)
    query_grads = jnp.einsum(
        "bhqk,bkhd->bqhd", grad_scores, head_keys, preferred_element_type=jnp.float32
    ).astype(jnp.bfloat16)
    key_window = jnp.einsum(
        "bhqk,bqhd->bkhd", grad_scores, head_queries, preferred_element_type=jnp.float32
    )
    kv_grad_window = jnp.stack([key_window, value_window], axis=2)
    kv_grads = (
        kv_grad_window[:, frames : 2 * frames]
        + from_neighbour(kv_grad_window[:, :frames].astype(jnp.bfloat16), "seq", -1).astype(
            jnp.float32
        )
        + from_neighbour(kv_grad_window[:, 2 * frames :].astype(jnp.bfloat16), "seq", 1).astype(
            jnp.float32
        )
    ).astype(jnp.bfloat16)
    grad_qkv = jnp.concatenate([query_grads[:, :, None], kv_grads], axis=2)
    grad_qkv = grad_qkv.reshape(batches, frames, 3 * model_width)
    flat_grad_qkv = grad_qkv.reshape(-1, 3 * model_width)
    grad_normed = jnp.dot(flat_grad_qkv, qkv_weight.T, preferred_element_type=jnp.float32)
    grad_normed = grad_normed.reshape(batches, frames, model_width)
    scaled = grad_normed * norm_gain
    grad_inputs = grad_hidden + inverse * (
        scaled
        - jnp.mean(scaled, axis=-1, keepdims=True)
        - unit_rows * jnp.mean(scaled * unit_rows, axis=-1, keepdims=True)
    )
    gain_sum = jnp.sum(grad_normed * unit_rows, axis=(0, 1))
    contract_rows = (((0,), (0,)), ((), ()))
    summed = staged_scatter(
        jnp.concatenate(
            [
                lax.dot_general(
                    flat_normed, flat_grad_qkv, contract_rows, preferred_element_type=jnp.float32
                ),
                lax.dot_general(
                    flat_attended,
                    flat_grad_hidden,
                    contract_rows,
                    preferred_element_type=jnp.float32,
                ),
            ],
            axis=1,
        )
    )
    small_sums = lax.psum((jnp.stack(kernel_rows), gain_sum), ("seq", "dp"))
    return (
        output,
        grad_inputs.astype(jnp.bfloat16),
        summed[:, : 3 * model_width] * factor,
        summed[:, 3 * model_width :] * factor,
        small_sums[0] * factor,
        small_sums[1] * factor,
    )


def solution(mesh):
    in_specs = (P("dp", "seq", None), P("dp", None), P(), P(), P(), P(), P("dp", "seq", None))
    out_specs = (
        P("dp", "seq", None),
        P("dp", "seq", None),
        P(("seq", "dp"), None),
        P(("seq", "dp"), None),
        P(),
        P(),
    )
    return jax.shard_map(local, mesh=mesh, in_specs=in_specs, out_specs=out_specs, check_vma=False)
```

```python
import jax
import jax.numpy as jnp
from jax import lax
from jax.sharding import PartitionSpec as P

HEADS = 16
MOST = 256


EPSILON = 1e-05
NEGATIVE = -1e30


def with_halo(shard, sides, width):
    for axis, dim in sides:
        size, length = (lax.axis_size(axis), shard.shape[dim])
        up = [(i, (i + 1) % size) for i in range(size - 1)]
        down = [(j, i) for i, j in up]
        last = lax.slice_in_dim(shard, length - width, length, axis=dim)
        initial = lax.slice_in_dim(shard, 0, width, axis=dim)
        before = lax.ppermute(last, axis, up)
        after = lax.ppermute(initial, axis, down)
        shard = jnp.concatenate([before, shard, after], axis=dim)
    return shard


def exchange_sum(value, axes):
    for axis in axes:
        size = lax.axis_size(axis)
        if size & (size - 1):
            value = lax.psum(value, axis)
            continue
        bit = 1
        while bit < size:
            value = value + lax.ppermute(value, axis, [(i, i ^ bit) for i in range(size)])
            bit *= 2
    return value


def staged_scatter(partial):
    partial = lax.psum_scatter(partial, "seq", scatter_dimension=0, tiled=True)
    return lax.psum_scatter(partial, "dp", scatter_dimension=0, tiled=True)


def segment_ids(positions, length_row, seq_length):
    ends = jnp.cumsum(length_row)
    inside = (positions >= 0) & (positions < seq_length)
    counted = jnp.sum((ends[None, :] <= positions[:, None]).astype(jnp.int32), axis=1)
    return jnp.where(inside, counted, -1)


def from_neighbour(shard, axis, step):
    size = lax.axis_size(axis)
    if step > 0:
        pairs = [(i, i + step) for i in range(size - step)]
    else:
        pairs = [(i - step, i) for i in range(size + step)]
    return lax.ppermute(shard, axis, pairs)


def local(inputs, lengths, norm_gain, qkv_weight, out_weight, kernel, cotangent):
    batches, frames, model_width = inputs.shape
    shards = lax.axis_size("seq")
    position = lax.axis_index("seq")
    seq_length = frames * shards
    head_dim = model_width // HEADS
    score_scale = head_dim ** (-0.5)
    conv_reach = kernel.shape[0] // 2
    factor = (batches * seq_length * lax.axis_size("dp")) ** (-0.5)
    first_frame = position * frames
    local_pos = first_frame + jnp.arange(frames, dtype=jnp.int32)
    segment_local = jnp.stack(
        [segment_ids(local_pos, lengths[batch_index], seq_length) for batch_index in range(batches)]
    )
    widened = inputs.astype(jnp.float32)
    average = jnp.mean(widened, axis=-1, keepdims=True)
    centred = widened - average
    inverse = lax.rsqrt(jnp.mean(centred * centred, axis=-1, keepdims=True) + EPSILON)
    unit_rows = centred * inverse
    normed = (unit_rows * norm_gain).astype(jnp.bfloat16)
    flat_normed = normed.reshape(-1, model_width)
    projected = jnp.dot(flat_normed, qkv_weight, preferred_element_type=jnp.float32).astype(
        jnp.bfloat16
    )
    projected = projected.reshape(batches, frames, 3 * model_width)
    proj5 = projected.reshape(batches, frames, 3, HEADS, head_dim)
    head_queries = proj5[:, :, 0]
    own_kv = proj5[:, :, 1:]
    kv_window = jnp.concatenate(
        [from_neighbour(own_kv, "seq", 1), own_kv, from_neighbour(own_kv, "seq", -1)], axis=1
    )
    head_keys = kv_window[:, :, 0]
    head_values = kv_window[:, :, 1]
    window_pos = first_frame - frames + jnp.arange(3 * frames, dtype=jnp.int32)
    segment_window = jnp.stack(
        [segment_ids(window_pos, lengths[batch_index], seq_length) for batch_index in range(batches)]
    )
    allowed = (segment_local[:, :, None] == segment_window[:, None, :])[:, None]
    scores = (
        jnp.einsum("bqhd,bkhd->bhqk", head_queries, head_keys, preferred_element_type=jnp.float32)
        * score_scale
    )
    scores = jnp.where(allowed, scores, NEGATIVE)
    row_max = jnp.max(scores, axis=-1, keepdims=True)
    exponent = jnp.where(allowed, jnp.exp(scores - row_max), 0.0)
    attn_probs = exponent / jnp.sum(exponent, axis=-1, keepdims=True)
    weights = attn_probs.astype(jnp.bfloat16)
    head_out = jnp.einsum(
        "bhqk,bkhd->bqhd", weights, head_values, preferred_element_type=jnp.float32
    ).astype(jnp.bfloat16)
    attended = head_out.reshape(batches, frames, model_width)
    flat_attended = attended.reshape(-1, model_width)
    attn_rows = jnp.dot(flat_attended, out_weight, preferred_element_type=jnp.float32)
    hidden = (widened + attn_rows.reshape(batches, frames, model_width)).astype(jnp.bfloat16)
    padded = with_halo(hidden, (("seq", 1),), conv_reach).astype(jnp.float32)
    ext_pos = first_frame - conv_reach + jnp.arange(frames + 2 * conv_reach, dtype=jnp.int32)
    segment_ext = jnp.stack(
        [segment_ids(ext_pos, lengths[batch_index], seq_length) for batch_index in range(batches)]
    )
    conv_sum = jnp.zeros((batches, frames, model_width), jnp.float32)
    for tap_index in range(kernel.shape[0]):
        same_seg = (segment_ext[:, tap_index : tap_index + frames] == segment_local)[..., None]
        conv_sum = conv_sum + jnp.where(
            same_seg, kernel[tap_index] * padded[:, tap_index : tap_index + frames], 0.0
        )
    gated = jax.nn.sigmoid(conv_sum)
    output = (hidden.astype(jnp.float32) + conv_sum * gated).astype(jnp.bfloat16)
    incoming = cotangent.astype(jnp.float32)
    grad_conv = incoming * gated * (1.0 + conv_sum * (1.0 - gated))
    grad_pad = with_halo(grad_conv.astype(jnp.bfloat16), (("seq", 1),), conv_reach).astype(
        grad_conv.dtype
    )
    grad_hidden = incoming
    kernel_rows = []
    for tap_index in range(kernel.shape[0]):
        back_index = 2 * conv_reach - tap_index
        same_back = (segment_ext[:, back_index : back_index + frames] == segment_local)[..., None]
        grad_hidden = grad_hidden + jnp.where(
            same_back, kernel[tap_index] * grad_pad[:, back_index : back_index + frames], 0.0
        )
        same_seg = (segment_ext[:, tap_index : tap_index + frames] == segment_local)[..., None]
        kernel_rows.append(
            jnp.sum(
                jnp.where(same_seg, grad_conv * padded[:, tap_index : tap_index + frames], 0.0),
                axis=(0, 1),
            )
        )
    grad_hidden_b = grad_hidden.astype(jnp.bfloat16)
    flat_grad_hidden = grad_hidden_b.reshape(-1, model_width)
    grad_attended = jnp.dot(
        flat_grad_hidden, out_weight.T, preferred_element_type=jnp.float32
    ).astype(jnp.bfloat16)
    grad_heads = grad_attended.reshape(batches, frames, HEADS, head_dim)
    row_delta = jnp.sum(
        grad_heads.astype(jnp.float32) * head_out.astype(jnp.float32), axis=-1
    ).transpose(0, 2, 1)[..., None]
    value_window = jnp.einsum(
        "bhqk,bqhd->bkhd", weights, grad_heads, preferred_element_type=jnp.float32
    )
    grad_probs = jnp.einsum(
        "bqhd,bkhd->bhqk", grad_heads, head_values, preferred_element_type=jnp.float32
    )
    grad_scores = (attn_probs * (grad_probs - row_delta) * score_scale).astype(jnp.bfloat16)
    query_grads = jnp.einsum(
        "bhqk,bkhd->bqhd", grad_scores, head_keys, preferred_element_type=jnp.float32
    ).astype(jnp.bfloat16)
    key_window = jnp.einsum(
        "bhqk,bqhd->bkhd", grad_scores, head_queries, preferred_element_type=jnp.float32
    )
    kv_grad_window = jnp.stack([key_window, value_window], axis=2)
    kv_grads = (
        kv_grad_window[:, frames : 2 * frames]
        + from_neighbour(kv_grad_window[:, :frames].astype(jnp.bfloat16), "seq", -1).astype(
            jnp.float32
        )
        + from_neighbour(kv_grad_window[:, 2 * frames :].astype(jnp.bfloat16), "seq", 1).astype(
            jnp.float32
        )
    ).astype(jnp.bfloat16)
    grad_qkv = jnp.concatenate([query_grads[:, :, None], kv_grads], axis=2)
    grad_qkv = grad_qkv.reshape(batches, frames, 3 * model_width)
    flat_grad_qkv = grad_qkv.reshape(-1, 3 * model_width)
    grad_normed = jnp.dot(flat_grad_qkv, qkv_weight.T, preferred_element_type=jnp.float32)
    grad_normed = grad_normed.reshape(batches, frames, model_width)
    scaled = grad_normed * norm_gain
    grad_inputs = grad_hidden + inverse * (
        scaled
        - jnp.mean(scaled, axis=-1, keepdims=True)
        - unit_rows * jnp.mean(scaled * unit_rows, axis=-1, keepdims=True)
    )
    gain_sum = jnp.sum(grad_normed * unit_rows, axis=(0, 1))
    contract_rows = (((0,), (0,)), ((), ()))
    summed = staged_scatter(
        jnp.concatenate(
            [
                lax.dot_general(
                    flat_normed, flat_grad_qkv, contract_rows, preferred_element_type=jnp.float32
                ),
                lax.dot_general(
                    flat_attended,
                    flat_grad_hidden,
                    contract_rows,
                    preferred_element_type=jnp.float32,
                ),
            ],
            axis=1,
        )
    )
    small_sums = (
        exchange_sum(jnp.stack(kernel_rows), ("seq", "dp")),
        exchange_sum(gain_sum.reshape(8, -1), ("seq", "dp")).reshape(-1),
    )
    return (
        output,
        grad_inputs.astype(jnp.bfloat16),
        summed[:, : 3 * model_width] * factor,
        summed[:, 3 * model_width :] * factor,
        small_sums[0] * factor,
        small_sums[1] * factor,
    )


def solution(mesh):
    in_specs = (P("dp", "seq", None), P("dp", None), P(), P(), P(), P(), P("dp", "seq", None))
    out_specs = (
        P("dp", "seq", None),
        P("dp", "seq", None),
        P(("seq", "dp"), None),
        P(("seq", "dp"), None),
        P(),
        P(),
    )
    return jax.shard_map(local, mesh=mesh, in_specs=in_specs, out_specs=out_specs, check_vma=False)
```

```python
import jax
import jax.numpy as jnp
from jax import lax
from jax.sharding import PartitionSpec as P

HEADS = 16
MOST = 256


EPSILON = 1e-05
NEGATIVE = -1e30


def with_halo(shard, sides, width):
    for axis, dim in sides:
        size, length = (lax.axis_size(axis), shard.shape[dim])
        up = [(i, (i + 1) % size) for i in range(size - 1)]
        down = [(j, i) for i, j in up]
        last = lax.slice_in_dim(shard, length - width, length, axis=dim)
        initial = lax.slice_in_dim(shard, 0, width, axis=dim)
        before = lax.ppermute(last, axis, up)
        after = lax.ppermute(initial, axis, down)
        shard = jnp.concatenate([before, shard, after], axis=dim)
    return shard


def exchange_sum(value, axes):
    for axis in axes:
        size = lax.axis_size(axis)
        if size & (size - 1):
            value = lax.psum(value, axis)
            continue
        bit = 1
        while bit < size:
            value = value + lax.ppermute(value, axis, [(i, i ^ bit) for i in range(size)])
            bit *= 2
    return value


def staged_scatter(partial):
    partial = lax.psum_scatter(partial, "seq", scatter_dimension=0, tiled=True)
    return lax.psum_scatter(partial, "dp", scatter_dimension=0, tiled=True)


def segment_ids(positions, length_row, seq_length):
    ends = jnp.cumsum(length_row)
    inside = (positions >= 0) & (positions < seq_length)
    counted = jnp.sum((ends[None, :] <= positions[:, None]).astype(jnp.int32), axis=1)
    return jnp.where(inside, counted, -1)


def from_neighbour(shard, axis, step):
    size = lax.axis_size(axis)
    if step > 0:
        pairs = [(i, i + step) for i in range(size - step)]
    else:
        pairs = [(i - step, i) for i in range(size + step)]
    return lax.ppermute(shard, axis, pairs)


def local(inputs, lengths, norm_gain, qkv_weight, out_weight, kernel, cotangent):
    batches, frames, model_width = inputs.shape
    shards = lax.axis_size("seq")
    position = lax.axis_index("seq")
    seq_length = frames * shards
    head_dim = model_width // HEADS
    score_scale = head_dim ** (-0.5)
    conv_reach = kernel.shape[0] // 2
    factor = (batches * seq_length * lax.axis_size("dp")) ** (-0.5)
    first_frame = position * frames
    local_pos = first_frame + jnp.arange(frames, dtype=jnp.int32)
    segment_local = jnp.stack(
        [segment_ids(local_pos, lengths[batch_index], seq_length) for batch_index in range(batches)]
    )
    widened = inputs.astype(jnp.float32)
    average = jnp.mean(widened, axis=-1, keepdims=True)
    centred = widened - average
    inverse = lax.rsqrt(jnp.mean(centred * centred, axis=-1, keepdims=True) + EPSILON)
    unit_rows = centred * inverse
    normed = (unit_rows * norm_gain).astype(jnp.bfloat16)
    flat_normed = normed.reshape(-1, model_width)
    projected = jnp.dot(flat_normed, qkv_weight, preferred_element_type=jnp.float32).astype(
        jnp.bfloat16
    )
    projected = projected.reshape(batches, frames, 3 * model_width)
    proj5 = projected.reshape(batches, frames, 3, HEADS, head_dim)
    head_queries = proj5[:, :, 0]
    own_kv = proj5[:, :, 1:]
    kv_window = jnp.concatenate(
        [from_neighbour(own_kv, "seq", 1), own_kv, from_neighbour(own_kv, "seq", -1)], axis=1
    )
    head_keys = kv_window[:, :, 0]
    head_values = kv_window[:, :, 1]
    window_pos = first_frame - frames + jnp.arange(3 * frames, dtype=jnp.int32)
    segment_window = jnp.stack(
        [segment_ids(window_pos, lengths[batch_index], seq_length) for batch_index in range(batches)]
    )
    allowed = (segment_local[:, :, None] == segment_window[:, None, :])[:, None]
    scores = (
        jnp.einsum("bqhd,bkhd->bhqk", head_queries, head_keys, preferred_element_type=jnp.float32)
        * score_scale
    )
    scores = jnp.where(allowed, scores, NEGATIVE)
    row_max = jnp.max(scores, axis=-1, keepdims=True)
    exponent = jnp.where(allowed, jnp.exp(scores - row_max), 0.0)
    attn_probs = exponent / jnp.sum(exponent, axis=-1, keepdims=True)
    weights = attn_probs.astype(jnp.bfloat16)
    head_out = jnp.einsum(
        "bhqk,bkhd->bqhd", weights, head_values, preferred_element_type=jnp.float32
    ).astype(jnp.bfloat16)
    attended = head_out.reshape(batches, frames, model_width)
    flat_attended = attended.reshape(-1, model_width)
    attn_rows = jnp.dot(flat_attended, out_weight, preferred_element_type=jnp.float32)
    hidden = (widened + attn_rows.reshape(batches, frames, model_width)).astype(jnp.bfloat16)
    padded = with_halo(hidden, (("seq", 1),), conv_reach).astype(jnp.float32)
    ext_pos = first_frame - conv_reach + jnp.arange(frames + 2 * conv_reach, dtype=jnp.int32)
    segment_ext = jnp.stack(
        [segment_ids(ext_pos, lengths[batch_index], seq_length) for batch_index in range(batches)]
    )
    conv_sum = jnp.zeros((batches, frames, model_width), jnp.float32)
    for tap_index in range(kernel.shape[0]):
        same_seg = (segment_ext[:, tap_index : tap_index + frames] == segment_local)[..., None]
        conv_sum = conv_sum + jnp.where(
            same_seg, kernel[tap_index] * padded[:, tap_index : tap_index + frames], 0.0
        )
    gated = jax.nn.sigmoid(conv_sum)
    output = (hidden.astype(jnp.float32) + conv_sum * gated).astype(jnp.bfloat16)
    incoming = cotangent.astype(jnp.float32)
    grad_conv = incoming * gated * (1.0 + conv_sum * (1.0 - gated))
    grad_pad = with_halo(grad_conv.astype(jnp.bfloat16), (("seq", 1),), conv_reach).astype(
        grad_conv.dtype
    )
    grad_hidden = incoming
    kernel_rows = []
    for tap_index in range(kernel.shape[0]):
        back_index = 2 * conv_reach - tap_index
        same_back = (segment_ext[:, back_index : back_index + frames] == segment_local)[..., None]
        grad_hidden = grad_hidden + jnp.where(
            same_back, kernel[tap_index] * grad_pad[:, back_index : back_index + frames], 0.0
        )
        same_seg = (segment_ext[:, tap_index : tap_index + frames] == segment_local)[..., None]
        kernel_rows.append(
            jnp.sum(
                jnp.where(same_seg, grad_conv * padded[:, tap_index : tap_index + frames], 0.0),
                axis=(0, 1),
            )
        )
    grad_hidden_b = grad_hidden.astype(jnp.bfloat16)
    flat_grad_hidden = grad_hidden_b.reshape(-1, model_width)
    grad_attended = jnp.dot(
        flat_grad_hidden, out_weight.T, preferred_element_type=jnp.float32
    ).astype(jnp.bfloat16)
    out_partial = lax.dot_general(
        flat_attended,
        flat_grad_hidden,
        (((0,), (0,)), ((), ())),
        preferred_element_type=jnp.float32,
    )
    grad_attended, out_partial = lax.optimization_barrier((grad_attended, out_partial))
    out_sum = staged_scatter(out_partial)
    grad_heads = grad_attended.reshape(batches, frames, HEADS, head_dim)
    row_delta = jnp.sum(
        grad_heads.astype(jnp.float32) * head_out.astype(jnp.float32), axis=-1
    ).transpose(0, 2, 1)[..., None]
    value_window = jnp.einsum(
        "bhqk,bqhd->bkhd", weights, grad_heads, preferred_element_type=jnp.float32
    )
    grad_probs = jnp.einsum(
        "bqhd,bkhd->bhqk", grad_heads, head_values, preferred_element_type=jnp.float32
    )
    grad_scores = (attn_probs * (grad_probs - row_delta) * score_scale).astype(jnp.bfloat16)
    query_grads = jnp.einsum(
        "bhqk,bkhd->bqhd", grad_scores, head_keys, preferred_element_type=jnp.float32
    ).astype(jnp.bfloat16)
    key_window = jnp.einsum(
        "bhqk,bqhd->bkhd", grad_scores, head_queries, preferred_element_type=jnp.float32
    )
    kv_grad_window = jnp.stack([key_window, value_window], axis=2)
    kv_grads = (
        kv_grad_window[:, frames : 2 * frames]
        + from_neighbour(kv_grad_window[:, :frames].astype(jnp.bfloat16), "seq", -1).astype(
            jnp.float32
        )
        + from_neighbour(kv_grad_window[:, 2 * frames :].astype(jnp.bfloat16), "seq", 1).astype(
            jnp.float32
        )
    ).astype(jnp.bfloat16)
    grad_qkv = jnp.concatenate([query_grads[:, :, None], kv_grads], axis=2)
    grad_qkv = grad_qkv.reshape(batches, frames, 3 * model_width)
    flat_grad_qkv = grad_qkv.reshape(-1, 3 * model_width)
    grad_normed = jnp.dot(flat_grad_qkv, qkv_weight.T, preferred_element_type=jnp.float32)
    grad_normed = grad_normed.reshape(batches, frames, model_width)
    scaled = grad_normed * norm_gain
    grad_inputs = grad_hidden + inverse * (
        scaled
        - jnp.mean(scaled, axis=-1, keepdims=True)
        - unit_rows * jnp.mean(scaled * unit_rows, axis=-1, keepdims=True)
    )
    gain_sum = jnp.sum(grad_normed * unit_rows, axis=(0, 1))
    contract_rows = (((0,), (0,)), ((), ()))
    qkv_partial = lax.dot_general(
        flat_normed, flat_grad_qkv, contract_rows, preferred_element_type=jnp.float32
    )
    qkv_partial, out_sum = lax.optimization_barrier((qkv_partial, out_sum))
    qkv_sum = staged_scatter(qkv_partial)
    small_sums = (
        exchange_sum(jnp.stack(kernel_rows), ("seq", "dp")),
        exchange_sum(gain_sum.reshape(8, -1), ("seq", "dp")).reshape(-1),
    )
    return (
        output,
        grad_inputs.astype(jnp.bfloat16),
        qkv_sum * factor,
        out_sum * factor,
        small_sums[0] * factor,
        small_sums[1] * factor,
    )


def solution(mesh):
    in_specs = (P("dp", "seq", None), P("dp", None), P(), P(), P(), P(), P("dp", "seq", None))
    out_specs = (
        P("dp", "seq", None),
        P("dp", "seq", None),
        P(("seq", "dp"), None),
        P(("seq", "dp"), None),
        P(),
        P(),
    )
    return jax.shard_map(local, mesh=mesh, in_specs=in_specs, out_specs=out_specs, check_vma=False)
```

```python
import jax
import jax.numpy as jnp
from jax import lax
from jax.sharding import PartitionSpec as P

HEADS = 16
MOST = 256


EPSILON = 1e-05
NEGATIVE = -1e30


def with_halo(shard, sides, width):
    for axis, dim in sides:
        size, length = (lax.axis_size(axis), shard.shape[dim])
        up = [(i, (i + 1) % size) for i in range(size - 1)]
        down = [(j, i) for i, j in up]
        last = lax.slice_in_dim(shard, length - width, length, axis=dim)
        initial = lax.slice_in_dim(shard, 0, width, axis=dim)
        before = lax.ppermute(last, axis, up)
        after = lax.ppermute(initial, axis, down)
        shard = jnp.concatenate([before, shard, after], axis=dim)
    return shard


def exchange_sum(value, axes):
    for axis in axes:
        size = lax.axis_size(axis)
        if size & (size - 1):
            value = lax.psum(value, axis)
            continue
        bit = 1
        while bit < size:
            value = value + lax.ppermute(value, axis, [(i, i ^ bit) for i in range(size)])
            bit *= 2
    return value


def staged_scatter(partial):
    partial = lax.psum_scatter(partial, "seq", scatter_dimension=0, tiled=True)
    return lax.psum_scatter(partial, "dp", scatter_dimension=0, tiled=True)


def segment_ids(positions, length_row, seq_length):
    ends = jnp.cumsum(length_row)
    inside = (positions >= 0) & (positions < seq_length)
    counted = jnp.sum((ends[None, :] <= positions[:, None]).astype(jnp.int32), axis=1)
    return jnp.where(inside, counted, -1)


def from_neighbour(shard, axis, step):
    size = lax.axis_size(axis)
    if step > 0:
        pairs = [(i, i + step) for i in range(size - step)]
    else:
        pairs = [(i - step, i) for i in range(size + step)]
    return lax.ppermute(shard, axis, pairs)


def local(inputs, lengths, norm_gain, qkv_weight, out_weight, kernel, cotangent):
    batches, frames, model_width = inputs.shape
    shards = lax.axis_size("seq")
    position = lax.axis_index("seq")
    seq_length = frames * shards
    head_dim = model_width // HEADS
    score_scale = head_dim ** (-0.5)
    conv_reach = kernel.shape[0] // 2
    factor = (batches * seq_length * lax.axis_size("dp")) ** (-0.5)
    first_frame = position * frames
    local_pos = first_frame + jnp.arange(frames, dtype=jnp.int32)
    segment_local = jnp.stack(
        [segment_ids(local_pos, lengths[batch_index], seq_length) for batch_index in range(batches)]
    )
    widened = inputs.astype(jnp.float32)
    average = jnp.mean(widened, axis=-1, keepdims=True)
    centred = widened - average
    inverse = lax.rsqrt(jnp.mean(centred * centred, axis=-1, keepdims=True) + EPSILON)
    unit_rows = centred * inverse
    normed = (unit_rows * norm_gain).astype(jnp.bfloat16)
    flat_normed = normed.reshape(-1, model_width)
    projected = jnp.dot(flat_normed, qkv_weight, preferred_element_type=jnp.float32).astype(
        jnp.bfloat16
    )
    projected = projected.reshape(batches, frames, 3 * model_width)
    proj5 = projected.reshape(batches, frames, 3, HEADS, head_dim)
    head_queries = proj5[:, :, 0]
    own_kv = proj5[:, :, 1:]
    kv_window = jnp.concatenate(
        [from_neighbour(own_kv, "seq", 1), own_kv, from_neighbour(own_kv, "seq", -1)], axis=1
    )
    head_keys = kv_window[:, :, 0]
    head_values = kv_window[:, :, 1]
    window_pos = first_frame - frames + jnp.arange(3 * frames, dtype=jnp.int32)
    segment_window = jnp.stack(
        [segment_ids(window_pos, lengths[batch_index], seq_length) for batch_index in range(batches)]
    )
    allowed = (segment_local[:, :, None] == segment_window[:, None, :])[:, None]
    scores = (
        jnp.einsum("bqhd,bkhd->bhqk", head_queries, head_keys, preferred_element_type=jnp.float32)
        * score_scale
    )
    scores = jnp.where(allowed, scores, NEGATIVE)
    row_max = jnp.max(scores, axis=-1, keepdims=True)
    exponent = jnp.where(allowed, jnp.exp(scores - row_max), 0.0)
    attn_probs = exponent / jnp.sum(exponent, axis=-1, keepdims=True)
    weights = attn_probs.astype(jnp.bfloat16)
    head_out = jnp.einsum(
        "bhqk,bkhd->bqhd", weights, head_values, preferred_element_type=jnp.float32
    ).astype(jnp.bfloat16)
    attended = head_out.reshape(batches, frames, model_width)
    flat_attended = attended.reshape(-1, model_width)
    attn_rows = jnp.dot(flat_attended, out_weight, preferred_element_type=jnp.float32)
    hidden = (widened + attn_rows.reshape(batches, frames, model_width)).astype(jnp.bfloat16)
    padded = with_halo(hidden, (("seq", 1),), conv_reach).astype(jnp.float32)
    ext_pos = first_frame - conv_reach + jnp.arange(frames + 2 * conv_reach, dtype=jnp.int32)
    segment_ext = jnp.stack(
        [segment_ids(ext_pos, lengths[batch_index], seq_length) for batch_index in range(batches)]
    )
    conv_sum = jnp.zeros((batches, frames, model_width), jnp.float32)
    for tap_index in range(kernel.shape[0]):
        same_seg = (segment_ext[:, tap_index : tap_index + frames] == segment_local)[..., None]
        conv_sum = conv_sum + jnp.where(
            same_seg, kernel[tap_index] * padded[:, tap_index : tap_index + frames], 0.0
        )
    gated = jax.nn.sigmoid(conv_sum)
    output = (hidden.astype(jnp.float32) + conv_sum * gated).astype(jnp.bfloat16)
    incoming = cotangent.astype(jnp.float32)
    grad_conv = incoming * gated * (1.0 + conv_sum * (1.0 - gated))
    grad_pad = with_halo(grad_conv.astype(jnp.bfloat16), (("seq", 1),), conv_reach).astype(
        grad_conv.dtype
    )
    grad_hidden = incoming
    for tap_index in range(kernel.shape[0]):
        back_index = 2 * conv_reach - tap_index
        same_back = (segment_ext[:, back_index : back_index + frames] == segment_local)[..., None]
        grad_hidden = grad_hidden + jnp.where(
            same_back, kernel[tap_index] * grad_pad[:, back_index : back_index + frames], 0.0
        )
    grad_hidden_b = grad_hidden.astype(jnp.bfloat16)
    flat_grad_hidden = grad_hidden_b.reshape(-1, model_width)
    grad_attended = jnp.dot(
        flat_grad_hidden, out_weight.T, preferred_element_type=jnp.float32
    ).astype(jnp.bfloat16)
    grad_heads = grad_attended.reshape(batches, frames, HEADS, head_dim)
    row_delta = jnp.sum(
        grad_heads.astype(jnp.float32) * head_out.astype(jnp.float32), axis=-1
    ).transpose(0, 2, 1)[..., None]
    value_window = jnp.einsum(
        "bhqk,bqhd->bkhd", weights, grad_heads, preferred_element_type=jnp.float32
    )
    grad_probs = jnp.einsum(
        "bqhd,bkhd->bhqk", grad_heads, head_values, preferred_element_type=jnp.float32
    )
    grad_scores = (attn_probs * (grad_probs - row_delta) * score_scale).astype(jnp.bfloat16)
    query_grads = jnp.einsum(
        "bhqk,bkhd->bqhd", grad_scores, head_keys, preferred_element_type=jnp.float32
    ).astype(jnp.bfloat16)
    key_window = jnp.einsum(
        "bhqk,bqhd->bkhd", grad_scores, head_queries, preferred_element_type=jnp.float32
    )
    kv_grad_window = jnp.stack([key_window, value_window], axis=2)
    kv_grads = (
        kv_grad_window[:, frames : 2 * frames]
        + from_neighbour(kv_grad_window[:, :frames].astype(jnp.bfloat16), "seq", -1).astype(
            jnp.float32
        )
        + from_neighbour(kv_grad_window[:, 2 * frames :].astype(jnp.bfloat16), "seq", 1).astype(
            jnp.float32
        )
    ).astype(jnp.bfloat16)
    grad_qkv = jnp.concatenate([query_grads[:, :, None], kv_grads], axis=2)
    grad_qkv = grad_qkv.reshape(batches, frames, 3 * model_width)
    flat_grad_qkv = grad_qkv.reshape(-1, 3 * model_width)
    grad_normed = jnp.dot(flat_grad_qkv, qkv_weight.T, preferred_element_type=jnp.float32)
    grad_normed = grad_normed.reshape(batches, frames, model_width)
    scaled = grad_normed * norm_gain
    grad_inputs = grad_hidden + inverse * (
        scaled
        - jnp.mean(scaled, axis=-1, keepdims=True)
        - unit_rows * jnp.mean(scaled * unit_rows, axis=-1, keepdims=True)
    )
    gain_sum = jnp.sum(grad_normed * unit_rows, axis=(0, 1))
    contract_rows = (((0,), (0,)), ((), ()))
    weight_partial = jnp.concatenate(
            [
                lax.dot_general(
                    flat_normed, flat_grad_qkv, contract_rows, preferred_element_type=jnp.float32
                ),
                lax.dot_general(
                    flat_attended,
                    flat_grad_hidden,
                    contract_rows,
                    preferred_element_type=jnp.float32,
                ),
            ],
            axis=1,
        )
    weight_partial, late_conv, late_padded = lax.optimization_barrier(
        (weight_partial, grad_conv, padded)
    )
    summed = staged_scatter(weight_partial)
    kernel_rows = []
    for tap_index in range(kernel.shape[0]):
        same_seg = (segment_ext[:, tap_index : tap_index + frames] == segment_local)[..., None]
        kernel_rows.append(
            jnp.sum(
                jnp.where(same_seg, late_conv * late_padded[:, tap_index : tap_index + frames], 0.0),
                axis=(0, 1),
            )
        )
    small_sums = (
        exchange_sum(jnp.stack(kernel_rows), ("seq", "dp")),
        exchange_sum(gain_sum.reshape(8, -1), ("seq", "dp")).reshape(-1),
    )
    return (
        output,
        grad_inputs.astype(jnp.bfloat16),
        summed[:, : 3 * model_width] * factor,
        summed[:, 3 * model_width :] * factor,
        small_sums[0] * factor,
        small_sums[1] * factor,
    )


def solution(mesh):
    in_specs = (P("dp", "seq", None), P("dp", None), P(), P(), P(), P(), P("dp", "seq", None))
    out_specs = (
        P("dp", "seq", None),
        P("dp", "seq", None),
        P(("seq", "dp"), None),
        P(("seq", "dp"), None),
        P(),
        P(),
    )
    return jax.shard_map(local, mesh=mesh, in_specs=in_specs, out_specs=out_specs, check_vma=False)
```

```python
import jax
import jax.numpy as jnp
from jax import lax
from jax.sharding import PartitionSpec as P

HEADS = 16
MOST = 256


EPSILON = 1e-05
NEGATIVE = -1e30


def with_halo(shard, sides, width):
    for axis, dim in sides:
        size, length = (lax.axis_size(axis), shard.shape[dim])
        up = [(i, (i + 1) % size) for i in range(size - 1)]
        down = [(j, i) for i, j in up]
        last = lax.slice_in_dim(shard, length - width, length, axis=dim)
        initial = lax.slice_in_dim(shard, 0, width, axis=dim)
        before = lax.ppermute(last, axis, up)
        after = lax.ppermute(initial, axis, down)
        shard = jnp.concatenate([before, shard, after], axis=dim)
    return shard


def exchange_sum(value, axes):
    for axis in axes:
        size = lax.axis_size(axis)
        if size & (size - 1):
            value = lax.psum(value, axis)
            continue
        bit = 1
        while bit < size:
            value = value + lax.ppermute(value, axis, [(i, i ^ bit) for i in range(size)])
            bit *= 2
    return value


def staged_scatter(partial):
    partial = lax.psum_scatter(partial, "seq", scatter_dimension=0, tiled=True)
    return lax.psum_scatter(partial, "dp", scatter_dimension=0, tiled=True)


def segment_ids(positions, length_row, seq_length):
    ends = jnp.cumsum(length_row)
    inside = (positions >= 0) & (positions < seq_length)
    counted = jnp.sum((ends[None, :] <= positions[:, None]).astype(jnp.int32), axis=1)
    return jnp.where(inside, counted, -1)


def from_neighbour(shard, axis, step):
    size = lax.axis_size(axis)
    if step > 0:
        pairs = [(i, i + step) for i in range(size - step)]
    else:
        pairs = [(i - step, i) for i in range(size + step)]
    return lax.ppermute(shard, axis, pairs)


def local(inputs, lengths, norm_gain, qkv_weight, out_weight, kernel, cotangent):
    batches, frames, model_width = inputs.shape
    shards = lax.axis_size("seq")
    position = lax.axis_index("seq")
    seq_length = frames * shards
    head_dim = model_width // HEADS
    score_scale = head_dim ** (-0.5)
    conv_reach = kernel.shape[0] // 2
    factor = (batches * seq_length * lax.axis_size("dp")) ** (-0.5)
    first_frame = position * frames
    local_pos = first_frame + jnp.arange(frames, dtype=jnp.int32)
    segment_local = jnp.stack(
        [segment_ids(local_pos, lengths[batch_index], seq_length) for batch_index in range(batches)]
    )
    widened = inputs.astype(jnp.float32)
    average = jnp.mean(widened, axis=-1, keepdims=True)
    centred = widened - average
    inverse = lax.rsqrt(jnp.mean(centred * centred, axis=-1, keepdims=True) + EPSILON)
    unit_rows = centred * inverse
    normed = (unit_rows * norm_gain).astype(jnp.bfloat16)
    flat_normed = normed.reshape(-1, model_width)
    projected = jnp.dot(flat_normed, qkv_weight, preferred_element_type=jnp.float32).astype(
        jnp.bfloat16
    )
    projected = projected.reshape(batches, frames, 3 * model_width)
    proj5 = projected.reshape(batches, frames, 3, HEADS, head_dim)
    head_queries = proj5[:, :, 0]
    own_kv = proj5[:, :, 1:]
    kv_window = jnp.concatenate(
        [from_neighbour(own_kv, "seq", 1), own_kv, from_neighbour(own_kv, "seq", -1)], axis=1
    )
    head_keys = kv_window[:, :, 0]
    head_values = kv_window[:, :, 1]
    window_pos = first_frame - frames + jnp.arange(3 * frames, dtype=jnp.int32)
    segment_window = jnp.stack(
        [segment_ids(window_pos, lengths[batch_index], seq_length) for batch_index in range(batches)]
    )
    allowed = (segment_local[:, :, None] == segment_window[:, None, :])[:, None]
    scores = (
        jnp.einsum("bqhd,bkhd->bhqk", head_queries, head_keys, preferred_element_type=jnp.float32)
        * score_scale
    )
    scores = jnp.where(allowed, scores, NEGATIVE)
    row_max = jnp.max(scores, axis=-1, keepdims=True)
    exponent = jnp.where(allowed, jnp.exp(scores - row_max), 0.0)
    attn_probs = exponent / jnp.sum(exponent, axis=-1, keepdims=True)
    weights = attn_probs.astype(jnp.bfloat16)
    head_out = jnp.einsum(
        "bhqk,bkhd->bqhd", weights, head_values, preferred_element_type=jnp.float32
    ).astype(jnp.bfloat16)
    attended = head_out.reshape(batches, frames, model_width)
    flat_attended = attended.reshape(-1, model_width)
    attn_rows = jnp.dot(flat_attended, out_weight, preferred_element_type=jnp.float32)
    hidden = (widened + attn_rows.reshape(batches, frames, model_width)).astype(jnp.bfloat16)
    padded = with_halo(hidden, (("seq", 1),), conv_reach).astype(jnp.float32)
    ext_pos = first_frame - conv_reach + jnp.arange(frames + 2 * conv_reach, dtype=jnp.int32)
    segment_ext = jnp.stack(
        [segment_ids(ext_pos, lengths[batch_index], seq_length) for batch_index in range(batches)]
    )
    conv_sum = jnp.zeros((batches, frames, model_width), jnp.float32)
    for tap_index in range(kernel.shape[0]):
        same_seg = (segment_ext[:, tap_index : tap_index + frames] == segment_local)[..., None]
        conv_sum = conv_sum + jnp.where(
            same_seg, kernel[tap_index] * padded[:, tap_index : tap_index + frames], 0.0
        )
    gated = jax.nn.sigmoid(conv_sum)
    incoming = cotangent.astype(jnp.float32)
    grad_conv = incoming * gated * (1.0 + conv_sum * (1.0 - gated))
    grad_pad = with_halo(grad_conv.astype(jnp.bfloat16), (("seq", 1),), conv_reach).astype(
        grad_conv.dtype
    )
    grad_hidden = incoming
    for tap_index in range(kernel.shape[0]):
        back_index = 2 * conv_reach - tap_index
        same_back = (segment_ext[:, back_index : back_index + frames] == segment_local)[..., None]
        grad_hidden = grad_hidden + jnp.where(
            same_back, kernel[tap_index] * grad_pad[:, back_index : back_index + frames], 0.0
        )
    grad_hidden_b = grad_hidden.astype(jnp.bfloat16)
    flat_grad_hidden = grad_hidden_b.reshape(-1, model_width)
    grad_attended = jnp.dot(
        flat_grad_hidden, out_weight.T, preferred_element_type=jnp.float32
    ).astype(jnp.bfloat16)
    grad_heads = grad_attended.reshape(batches, frames, HEADS, head_dim)
    row_delta = jnp.sum(
        grad_heads.astype(jnp.float32) * head_out.astype(jnp.float32), axis=-1
    ).transpose(0, 2, 1)[..., None]
    value_window = jnp.einsum(
        "bhqk,bqhd->bkhd", weights, grad_heads, preferred_element_type=jnp.float32
    )
    grad_probs = jnp.einsum(
        "bqhd,bkhd->bhqk", grad_heads, head_values, preferred_element_type=jnp.float32
    )
    grad_scores = (attn_probs * (grad_probs - row_delta) * score_scale).astype(jnp.bfloat16)
    query_grads = jnp.einsum(
        "bhqk,bkhd->bqhd", grad_scores, head_keys, preferred_element_type=jnp.float32
    ).astype(jnp.bfloat16)
    key_window = jnp.einsum(
        "bhqk,bqhd->bkhd", grad_scores, head_queries, preferred_element_type=jnp.float32
    )
    kv_grad_window = jnp.stack([key_window, value_window], axis=2)
    kv_grads = (
        kv_grad_window[:, frames : 2 * frames]
        + from_neighbour(kv_grad_window[:, :frames].astype(jnp.bfloat16), "seq", -1).astype(
            jnp.float32
        )
        + from_neighbour(kv_grad_window[:, 2 * frames :].astype(jnp.bfloat16), "seq", 1).astype(
            jnp.float32
        )
    ).astype(jnp.bfloat16)
    grad_qkv = jnp.concatenate([query_grads[:, :, None], kv_grads], axis=2)
    grad_qkv = grad_qkv.reshape(batches, frames, 3 * model_width)
    flat_grad_qkv = grad_qkv.reshape(-1, 3 * model_width)
    grad_normed = jnp.dot(flat_grad_qkv, qkv_weight.T, preferred_element_type=jnp.float32)
    grad_normed = grad_normed.reshape(batches, frames, model_width)
    scaled = grad_normed * norm_gain
    grad_inputs = grad_hidden + inverse * (
        scaled
        - jnp.mean(scaled, axis=-1, keepdims=True)
        - unit_rows * jnp.mean(scaled * unit_rows, axis=-1, keepdims=True)
    )
    gain_sum = jnp.sum(grad_normed * unit_rows, axis=(0, 1))
    contract_rows = (((0,), (0,)), ((), ()))
    weight_partial = jnp.concatenate(
            [
                lax.dot_general(
                    flat_normed, flat_grad_qkv, contract_rows, preferred_element_type=jnp.float32
                ),
                lax.dot_general(
                    flat_attended,
                    flat_grad_hidden,
                    contract_rows,
                    preferred_element_type=jnp.float32,
                ),
            ],
            axis=1,
        )
    weight_partial, late_conv, late_padded, late_hidden, late_sum = lax.optimization_barrier(
        (weight_partial, grad_conv, padded, hidden, conv_sum)
    )
    output = (
        late_hidden.astype(jnp.float32) + late_sum * jax.nn.sigmoid(late_sum)
    ).astype(jnp.bfloat16)
    summed = staged_scatter(weight_partial)
    kernel_rows = []
    for tap_index in range(kernel.shape[0]):
        same_seg = (segment_ext[:, tap_index : tap_index + frames] == segment_local)[..., None]
        kernel_rows.append(
            jnp.sum(
                jnp.where(same_seg, late_conv * late_padded[:, tap_index : tap_index + frames], 0.0),
                axis=(0, 1),
            )
        )
    small_sums = (
        exchange_sum(jnp.stack(kernel_rows), ("seq", "dp")),
        exchange_sum(gain_sum.reshape(8, -1), ("seq", "dp")).reshape(-1),
    )
    return (
        output,
        grad_inputs.astype(jnp.bfloat16),
        summed[:, : 3 * model_width] * factor,
        summed[:, 3 * model_width :] * factor,
        small_sums[0] * factor,
        small_sums[1] * factor,
    )


def solution(mesh):
    in_specs = (P("dp", "seq", None), P("dp", None), P(), P(), P(), P(), P("dp", "seq", None))
    out_specs = (
        P("dp", "seq", None),
        P("dp", "seq", None),
        P(("seq", "dp"), None),
        P(("seq", "dp"), None),
        P(),
        P(),
    )
    return jax.shard_map(local, mesh=mesh, in_specs=in_specs, out_specs=out_specs, check_vma=False)
```
